1024 devices in a mesh: lat: 16 (over z_lo, core), lon: 64 (over z_hi, y, x).
Axes of the slice: x: 4, y: 8, z: 16 (z_hi: 2, z_lo: 8; z = z_hi * 8 + z_lo), core: 2. Of those that a mesh axis runs over, the one named last changes fastest.
Arguments:
- state: float32 [128, 1152, 192], P('lat', 'lon'), may hold values from -6 to 6
- courant_east: float32 [128, 1152, 192], P('lat', 'lon'), may hold values from -0.9 to 0.9
- courant_north: float32 [128, 1152, 192], P('lat', 'lon'), may hold values from -0.9 to 0.9
- cutoff: int32 [128], P('lat'), may hold values from 1 to 568, as said below
- filter_mask: int32 [128], P('lat'), may hold values from 0 to 1, as said below
Outputs:
- advanced: float32 [128, 1152, 192], P('lat', 'lon')
The draws below stay inside these ranges and needn't reach their ends.
Inputs may be any that keep to these rules, and one draw needn't show every extreme that they name: Row j's cutoff is at most 144 + 431 * d // 64, where d = min(j, 127 - j), and equals that bound on the two rows with d = 63; the two rows with d = 0 have cutoff 1. filter_mask is 0 on every row j with min(j, 127 - j) >= 32, and 1 on row 0.
All inputs are finite; a program needn't handle non-finite values.
Results may differ from the reference program's by a relative error of at most 0.00012.
Values sent between devices are 32-bit elements; how exact they have to be, the bound alone decides.
No kernel may reach another device: no remote copies, remote signals or barrier semaphores. Data moves between devices by JAX's collectives and lax.ppermute only.
A program may use at most 32 MiB of HBM per device.

```python
import math
import jax
import jax.numpy as jnp

NLAT = 128
NLON = 1152
COMP = 192


def draw_cutoff(key, part):
    row_ids = jnp.arange(NLAT, dtype=jnp.int32)
    to_pole = jnp.minimum(row_ids, NLAT - 1 - row_ids)
    ceiling = NLON // 8 + (NLON // 2 - 1 - NLON // 8) * to_pole // (NLAT // 2)
    drawn = jax.random.randint(jax.random.fold_in(key, 11), (NLAT,), 1, ceiling + 1, dtype=jnp.int32)
    drawn = jnp.where(to_pole == NLAT // 2 - 1, ceiling, drawn)
    return jnp.where(to_pole == 0, jnp.ones_like(drawn), drawn)


def draw_filter_mask(key, part):
    row_ids = jnp.arange(NLAT, dtype=jnp.int32)
    to_pole = jnp.minimum(row_ids, NLAT - 1 - row_ids)
    coins = jax.random.randint(jax.random.fold_in(key, 23), (NLAT,), 0, 2, dtype=jnp.int32)
    inside = jnp.where(to_pole < NLAT // 4, coins, jnp.zeros_like(coins))
    return jnp.where(row_ids == 0, jnp.ones_like(inside), inside)


def shard_levels(own_key, dims, pieces, smallest, high):
    factor_of = 1.0
    for axis_at, shards_of in pieces:
        draws = jax.random.uniform(jax.random.fold_in(jax.random.fold_in(own_key, 6), axis_at), (shards_of,), jnp.float32, smallest / len(pieces), high / len(pieces))
        factor_of = factor_of * jnp.repeat(jnp.exp(draws), dims[axis_at] // shards_of).reshape((-1,) + (1,) * (len(dims) - 1 - axis_at))
    return factor_of


def scatter_about(stream_key, shape, deviation, bound, split=(), held_as=jnp.bfloat16):
    array = jax.random.normal(stream_key, shape, jnp.float32) * deviation
    if len(split) > 0:
        array = shard_levels(stream_key, shape, split, -0.22, 0.18) * array
    return jnp.clip(array, min=-bound, max=bound).astype(held_as)


def setup_inputs(seed: int = 0) -> dict:
    key_of = jax.random.split(jax.random.key(seed), 6)
    return {
        "state": scatter_about(key_of[0], (NLAT, NLON, COMP), 1.0, 6.0, ((0, 16), (1, 64)), jnp.float32),
        "courant_east": jnp.clip(jax.random.uniform(key_of[1], (NLAT, NLON, COMP), jnp.float32, -0.9, 0.9) * shard_levels(key_of[1], (NLAT, NLON, COMP), ((0, 16), (1, 64)), -0.4, 0.0), -0.9, 0.9),
        "courant_north": jnp.clip(jax.random.uniform(key_of[2], (NLAT, NLON, COMP), jnp.float32, -0.9, 0.9) * shard_levels(key_of[2], (NLAT, NLON, COMP), ((0, 16), (1, 64)), -0.4, 0.0), -0.9, 0.9),
        "cutoff": draw_cutoff(jax.random.fold_in(key_of[5], 71), 0),
        "filter_mask": draw_filter_mask(jax.random.fold_in(key_of[5], 71), 0),
    }


def face_flux(far_lo, near_lo, near_hi, far_hi, courant):
    centred = (7.0 * (near_lo + near_hi) - (far_lo + far_hi)) / 12.0
    return courant * centred - 0.5 * jnp.abs(courant) * (near_hi - near_lo)


def reference(state, courant_east, courant_north, cutoff, filter_mask):
    spectra = jnp.fft.rfft(state, axis=1)
    waves = jnp.arange(NLON // 2 + 1, dtype=jnp.int32)
    allowed = waves[None, :] <= cutoff[:, None]
    filtered = jnp.fft.irfft(jnp.where(allowed[:, :, None], spectra, 0.0), n=NLON, axis=1).astype(jnp.float32)
    smooth = jnp.where(filter_mask[:, None, None] == 1, filtered, state)
    south = jnp.roll(smooth[:2][::-1], NLON // 2, axis=1)
    north = jnp.roll(smooth[::-1][:2], NLON // 2, axis=1)
    merid_p = jnp.concatenate([south, smooth, north], axis=0)
    zonal_p = jnp.concatenate([smooth[:, -2:], smooth, smooth[:, :2]], axis=1)
    zonal_c = jnp.concatenate([courant_east[:, -1:], courant_east], axis=1)
    east = face_flux(zonal_p[:, 0:NLON + 1], zonal_p[:, 1:NLON + 2], zonal_p[:, 2:NLON + 3], zonal_p[:, 3:NLON + 4], zonal_c)
    zonal = -(east[:, 1:] - east[:, :-1])
    merid_c = jnp.concatenate([jnp.zeros_like(courant_north[:1]), courant_north], axis=0)
    north_flux = face_flux(merid_p[0:NLAT + 1], merid_p[1:NLAT + 2], merid_p[2:NLAT + 3], merid_p[3:NLAT + 4], merid_c)
    face_rows = jnp.arange(-1, NLAT, dtype=jnp.int32)
    cos_face = jnp.sin(jnp.minimum(face_rows + 1, NLAT - 1 - face_rows).astype(jnp.float32) * (math.pi / NLAT))
    cell_rows = face_rows[1:]
    cos_cell = jnp.sin((jnp.minimum(cell_rows, NLAT - 1 - cell_rows).astype(jnp.float32) + 0.5) * (math.pi / NLAT))
    weighted = cos_face[:, None, None] * north_flux
    meridional = -(weighted[1:] - weighted[:-1]) / cos_cell[:, None, None]
    return smooth + zonal + meridional
```

```python
import math

import jax
import jax.numpy as jnp
from jax import lax
from jax.sharding import PartitionSpec as P


def shifted_from(block, axis, distance):
    count = lax.axis_size(axis)
    route = [(i, (i + distance) % count) for i in range(count)]
    return lax.ppermute(block, axis, route)


def face_flux(far_lo, near_lo, near_hi, far_hi, courant):
    centred = (7.0 * (near_lo + near_hi) - (far_lo + far_hi)) / 12.0
    return courant * centred - 0.5 * jnp.abs(courant) * (near_hi - near_lo)


def build_table(n_full, n_waves):
    points = jnp.arange(n_full, dtype=jnp.int32)
    waves = jnp.arange(n_waves, dtype=jnp.int32)
    phase = points[:, None] * waves[None, :] % n_full
    angle = phase.astype(jnp.float32) * (2.0 * math.pi / n_full)
    return jnp.concatenate([jnp.cos(angle), jnp.sin(angle)], axis=1)


def local(state, courant_east, courant_north, cutoff_all, mask_all):
    n_rows, n_cols, n_comp = state.shape
    lon_count = lax.axis_size("lon")
    lat_count = lax.axis_size("lat")
    lat_index = lax.axis_index("lat")
    n_full = n_cols * lon_count
    n_lat = n_rows * lat_count
    half = n_full // 2
    group = n_comp // lon_count

    top = n_full // 8 + (half - 1 - n_full // 8) * (n_lat // 4 - 1) // (n_lat // 2)
    n_waves = min(top, half - 1) + 1

    from_south = shifted_from(
        jnp.concatenate([state[-2:], courant_north[-1:]], axis=0), "lat", 1
    )
    from_north = shifted_from(state[:2], "lat", -1)
    east_halo = shifted_from(courant_east[:, -1:], "lon", 1)

    rows_ext = jnp.concatenate([from_south[:2], state, from_north], axis=0)
    n_ext = n_rows + 4
    lines = lax.all_to_all(rows_ext, "lon", split_axis=2, concat_axis=1, tiled=True)

    fourier = build_table(n_full, n_waves)
    waves = jnp.arange(n_waves, dtype=jnp.int32)
    weights = jnp.where(waves == 0, 1.0 / n_full, 2.0 / n_full).astype(jnp.float32)
    cut_pad = jnp.pad(cutoff_all, (2, 2))
    mask_pad = jnp.pad(mask_all, (2, 2))
    start = lat_index * n_rows
    cut_ext = lax.dynamic_slice_in_dim(cut_pad, start, n_ext)
    mask_ext = lax.dynamic_slice_in_dim(mask_pad, start, n_ext)
    kept = jnp.where(waves[None, :] <= cut_ext[:, None], weights[None, :], 0.0)
    kept_both = jnp.concatenate([kept, kept], axis=1)
    coeffs = lax.dot_general(
        lines, fourier, (((1,), (0,)), ((), ())), precision=lax.Precision.HIGHEST
    )
    coeffs = coeffs * kept_both[:, None, :]
    synth = lax.dot_general(
        coeffs, fourier, (((2,), (1,)), ((), ())), precision=lax.Precision.HIGHEST
    )
    filtered = jnp.transpose(synth, (0, 2, 1))
    smooth = jnp.where(mask_ext[:, None, None] == 1, filtered, lines)

    south_pole = jnp.roll(smooth[3:1:-1], half, axis=1)
    north_pole = jnp.roll(smooth[n_ext - 3 : n_ext - 5 : -1], half, axis=1)
    low = jnp.where(lat_index == 0, south_pole, smooth[:2])
    high = jnp.where(lat_index == lat_count - 1, north_pole, smooth[-2:])
    smooth = jnp.concatenate([low, smooth[2:-2], high], axis=0)

    tiles = smooth.reshape(n_ext, lon_count, n_cols, group)
    left = jnp.roll(tiles[:, :, -2:], 1, axis=1)
    right = jnp.roll(tiles[:, :, :2], -1, axis=1)
    windows = jnp.concatenate([left, tiles, right], axis=2)
    windows = jnp.transpose(windows, (1, 0, 2, 3))
    back = lax.all_to_all(windows, "lon", split_axis=0, concat_axis=0, tiled=True)
    ext = jnp.transpose(back, (1, 2, 0, 3)).reshape(n_ext, n_cols + 4, n_comp)

    zonal_p = ext[2:-2]
    zonal_c = jnp.concatenate([east_halo, courant_east], axis=1)
    east = face_flux(
        zonal_p[:, 0 : n_cols + 1],
        zonal_p[:, 1 : n_cols + 2],
        zonal_p[:, 2 : n_cols + 3],
        zonal_p[:, 3 : n_cols + 4],
        zonal_c,
    )
    zonal = -(east[:, 1:] - east[:, :-1])

    merid_p = ext[:, 2:-2]
    south_c = jnp.where(lat_index == 0, 0.0, from_south[2:])
    merid_c = jnp.concatenate([south_c, courant_north], axis=0)
    north_flux = face_flux(
        merid_p[0 : n_rows + 1],
        merid_p[1 : n_rows + 2],
        merid_p[2 : n_rows + 3],
        merid_p[3 : n_rows + 4],
        merid_c,
    )
    face_rows = lat_index * n_rows + jnp.arange(-1, n_rows, dtype=jnp.int32)
    cos_face = jnp.sin(
        jnp.minimum(face_rows + 1, n_lat - 1 - face_rows).astype(jnp.float32) * (math.pi / n_lat)
    )
    cell_rows = face_rows[1:]
    cos_cell = jnp.sin(
        (jnp.minimum(cell_rows, n_lat - 1 - cell_rows).astype(jnp.float32) + 0.5)
        * (math.pi / n_lat)
    )
    weighted = cos_face[:, None, None] * north_flux
    meridional = -(weighted[1:] - weighted[:-1]) / cos_cell[:, None, None]
    return zonal_p[:, 2:-2] + zonal + meridional


def solution(mesh):
    placed = (
        P("lat", "lon", None),
        P("lat", "lon", None),
        P("lat", "lon", None),
        P(None),
        P(None),
    )
    return jax.shard_map(
        local, mesh=mesh, in_specs=placed, out_specs=P("lat", "lon", None), check_vma=False
    )
```

```python
import math

import jax
import jax.numpy as jnp
from jax import lax
from jax.sharding import PartitionSpec as P


def shifted_from(block, axis, distance):
    count = lax.axis_size(axis)
    route = [(i, (i + distance) % count) for i in range(count)]
    return lax.ppermute(block, axis, route)


def face_flux(far_lo, near_lo, near_hi, far_hi, courant):
    centred = (7.0 * (near_lo + near_hi) - (far_lo + far_hi)) / 12.0
    return courant * centred - 0.5 * jnp.abs(courant) * (near_hi - near_lo)


def build_table(n_full, n_waves):
    points = jnp.arange(n_full, dtype=jnp.int32)
    waves = jnp.arange(n_waves, dtype=jnp.int32)
    phase = points[:, None] * waves[None, :] % n_full
    angle = phase.astype(jnp.float32) * (2.0 * math.pi / n_full)
    return jnp.concatenate([jnp.cos(angle), jnp.sin(angle)], axis=1)


def local(state, courant_east, courant_north, cutoff_all, mask_all):
    n_rows, n_cols, n_comp = state.shape
    lon_count = lax.axis_size("lon")
    lat_count = lax.axis_size("lat")
    lat_index = lax.axis_index("lat")
    n_full = n_cols * lon_count
    n_lat = n_rows * lat_count
    half = n_full // 2
    group = n_comp // lon_count

    top = n_full // 8 + (half - 1 - n_full // 8) * (n_lat // 4 - 1) // (n_lat // 2)
    n_waves = min(top, half - 1) + 1

    def row_info(sel):
        whole = jnp.concatenate([cutoff_all[sel], mask_all[sel]]).astype(jnp.float32)
        blank = jnp.zeros((1, n_cols, n_comp), jnp.float32)
        return blank.at[0, 0, : whole.shape[0]].set(whole)

    from_south = shifted_from(
        jnp.concatenate(
            [state[-2:], courant_north[-1:], row_info(slice(n_rows - 2, n_rows))], axis=0
        ),
        "lat",
        1,
    )
    from_north = shifted_from(
        jnp.concatenate([state[:2], row_info(slice(0, 2))], axis=0), "lat", -1
    )
    east_halo = shifted_from(courant_east[:, -1:], "lon", 1)

    rows_ext = jnp.concatenate([from_south[:2], state, from_north[:2]], axis=0)
    n_ext = n_rows + 4
    lines = lax.all_to_all(rows_ext, "lon", split_axis=2, concat_axis=1, tiled=True)

    fourier = build_table(n_full, n_waves)
    waves = jnp.arange(n_waves, dtype=jnp.int32)
    weights = jnp.where(waves == 0, 1.0 / n_full, 2.0 / n_full).astype(jnp.float32)
    info_s = from_south[3, 0, :4].astype(jnp.int32)
    info_n = from_north[2, 0, :4].astype(jnp.int32)
    cut_ext = jnp.concatenate([info_s[:2], cutoff_all, info_n[:2]])
    mask_ext = jnp.concatenate([info_s[2:], mask_all, info_n[2:]])
    kept = jnp.where(waves[None, :] <= cut_ext[:, None], weights[None, :], 0.0)
    kept_both = jnp.concatenate([kept, kept], axis=1)
    coeffs = lax.dot_general(
        lines, fourier, (((1,), (0,)), ((), ())), precision=lax.Precision.HIGHEST
    )
    coeffs = coeffs * kept_both[:, None, :]
    synth = lax.dot_general(
        coeffs, fourier, (((2,), (1,)), ((), ())), precision=lax.Precision.HIGHEST
    )
    filtered = jnp.transpose(synth, (0, 2, 1))
    smooth = jnp.where(mask_ext[:, None, None] == 1, filtered, lines)

    south_pole = jnp.roll(smooth[3:1:-1], half, axis=1)
    north_pole = jnp.roll(smooth[n_ext - 3 : n_ext - 5 : -1], half, axis=1)
    low = jnp.where(lat_index == 0, south_pole, smooth[:2])
    high = jnp.where(lat_index == lat_count - 1, north_pole, smooth[-2:])
    smooth = jnp.concatenate([low, smooth[2:-2], high], axis=0)

    tiles = smooth.reshape(n_ext, lon_count, n_cols, group)
    left = jnp.roll(tiles[:, :, -2:], 1, axis=1)
    right = jnp.roll(tiles[:, :, :2], -1, axis=1)
    windows = jnp.concatenate([left, tiles, right], axis=2)
    windows = windows.reshape(n_ext, lon_count * (n_cols + 4), group)
    ext = lax.all_to_all(windows, "lon", split_axis=1, concat_axis=2, tiled=True)

    zonal_p = ext[2:-2]
    zonal_c = jnp.concatenate([east_halo, courant_east], axis=1)
    east = face_flux(
        zonal_p[:, 0 : n_cols + 1],
        zonal_p[:, 1 : n_cols + 2],
        zonal_p[:, 2 : n_cols + 3],
        zonal_p[:, 3 : n_cols + 4],
        zonal_c,
    )
    zonal = -(east[:, 1:] - east[:, :-1])

    merid_p = ext[:, 2:-2]
    south_c = jnp.where(lat_index == 0, 0.0, from_south[2:3])
    merid_c = jnp.concatenate([south_c, courant_north], axis=0)
    north_flux = face_flux(
        merid_p[0 : n_rows + 1],
        merid_p[1 : n_rows + 2],
        merid_p[2 : n_rows + 3],
        merid_p[3 : n_rows + 4],
        merid_c,
    )
    face_rows = lat_index * n_rows + jnp.arange(-1, n_rows, dtype=jnp.int32)
    cos_face = jnp.sin(
        jnp.minimum(face_rows + 1, n_lat - 1 - face_rows).astype(jnp.float32) * (math.pi / n_lat)
    )
    cell_rows = face_rows[1:]
    cos_cell = jnp.sin(
        (jnp.minimum(cell_rows, n_lat - 1 - cell_rows).astype(jnp.float32) + 0.5)
        * (math.pi / n_lat)
    )
    weighted = cos_face[:, None, None] * north_flux
    meridional = -(weighted[1:] - weighted[:-1]) / cos_cell[:, None, None]
    return zonal_p[:, 2:-2] + zonal + meridional


def solution(mesh):
    placed = (
        P("lat", "lon", None),
        P("lat", "lon", None),
        P("lat", "lon", None),
        P("lat"),
        P("lat"),
    )
    return jax.shard_map(
        local, mesh=mesh, in_specs=placed, out_specs=P("lat", "lon", None), check_vma=False
    )
```

```python
import math

import jax
import jax.numpy as jnp
from jax import lax
from jax.sharding import PartitionSpec as P


def shifted_from(block, axis, distance):
    count = lax.axis_size(axis)
    route = [(i, (i + distance) % count) for i in range(count)]
    return lax.ppermute(block, axis, route)


def face_flux(far_lo, near_lo, near_hi, far_hi, courant):
    centred = (7.0 * (near_lo + near_hi) - (far_lo + far_hi)) / 12.0
    return courant * centred - 0.5 * jnp.abs(courant) * (near_hi - near_lo)


def build_table(n_full, n_waves):
    points = jnp.arange(n_full, dtype=jnp.int32)
    waves = jnp.arange(n_waves, dtype=jnp.int32)
    phase = points[:, None] * waves[None, :] % n_full
    angle = phase.astype(jnp.float32) * (2.0 * math.pi / n_full)
    return jnp.concatenate([jnp.cos(angle), jnp.sin(angle)], axis=1)


def local(state, courant_east, courant_north, cutoff, filter_mask):
    n_rows, n_cols, n_comp = state.shape
    lon_count = lax.axis_size("lon")
    lat_count = lax.axis_size("lat")
    lat_index = lax.axis_index("lat")
    n_full = n_cols * lon_count
    n_lat = n_rows * lat_count
    half = n_full // 2

    top = n_full // 8 + (half - 1 - n_full // 8) * (n_lat // 4 - 1) // (n_lat // 2)
    n_waves = min(top, half - 1) + 1

    east_halo = shifted_from(courant_east[:, -1:], "lon", 1)
    north_halo = shifted_from(courant_north[-1:], "lat", 1)

    lines = lax.all_to_all(state, "lon", split_axis=2, concat_axis=1, tiled=True)
    fourier = build_table(n_full, n_waves)
    waves = jnp.arange(n_waves, dtype=jnp.int32)
    weights = jnp.where(waves == 0, 1.0 / n_full, 2.0 / n_full).astype(jnp.float32)
    kept = jnp.where(waves[None, :] <= cutoff[:, None], weights[None, :], 0.0)
    kept_both = jnp.concatenate([kept, kept], axis=1)
    coeffs = lax.dot_general(
        lines, fourier, (((1,), (0,)), ((), ())), precision=lax.Precision.HIGHEST
    )
    coeffs = coeffs * kept_both[:, None, :]
    synth = lax.dot_general(
        coeffs, fourier, (((2,), (1,)), ((), ())), precision=lax.Precision.HIGHEST
    )
    filtered = jnp.transpose(synth, (0, 2, 1))
    merged = jnp.where(filter_mask[:, None, None] == 1, filtered, lines)
    smooth = lax.all_to_all(merged, "lon", split_axis=1, concat_axis=2, tiled=True)

    from_south = shifted_from(smooth[-2:], "lat", 1)
    from_north = shifted_from(smooth[:2], "lat", -1)
    from_west = shifted_from(smooth[:, -2:], "lon", 1)
    from_east = shifted_from(smooth[:, :2], "lon", -1)
    poles = jnp.concatenate([smooth[1::-1], smooth[:-3:-1]], axis=0)
    partner = shifted_from(poles, "lon", lon_count // 2)

    zonal_p = jnp.concatenate([from_west, smooth, from_east], axis=1)
    zonal_c = jnp.concatenate([east_halo, courant_east], axis=1)
    east = face_flux(
        zonal_p[:, 0 : n_cols + 1],
        zonal_p[:, 1 : n_cols + 2],
        zonal_p[:, 2 : n_cols + 3],
        zonal_p[:, 3 : n_cols + 4],
        zonal_c,
    )
    zonal = -(east[:, 1:] - east[:, :-1])

    south = jnp.where(lat_index == 0, partner[:2], from_south)
    north = jnp.where(lat_index == lat_count - 1, partner[2:], from_north)
    merid_p = jnp.concatenate([south, smooth, north], axis=0)
    south_c = jnp.where(lat_index == 0, 0.0, north_halo)
    merid_c = jnp.concatenate([south_c, courant_north], axis=0)
    north_flux = face_flux(
        merid_p[0 : n_rows + 1],
        merid_p[1 : n_rows + 2],
        merid_p[2 : n_rows + 3],
        merid_p[3 : n_rows + 4],
        merid_c,
    )
    face_rows = lat_index * n_rows + jnp.arange(-1, n_rows, dtype=jnp.int32)
    cos_face = jnp.sin(
        jnp.minimum(face_rows + 1, n_lat - 1 - face_rows).astype(jnp.float32) * (math.pi / n_lat)
    )
    cell_rows = face_rows[1:]
    cos_cell = jnp.sin(
        (jnp.minimum(cell_rows, n_lat - 1 - cell_rows).astype(jnp.float32) + 0.5)
        * (math.pi / n_lat)
    )
    weighted = cos_face[:, None, None] * north_flux
    meridional = -(weighted[1:] - weighted[:-1]) / cos_cell[:, None, None]
    return smooth + zonal + meridional


def solution(mesh):
    placed = (
        P("lat", "lon", None),
        P("lat", "lon", None),
        P("lat", "lon", None),
        P("lat"),
        P("lat"),
    )
    return jax.shard_map(
        local, mesh=mesh, in_specs=placed, out_specs=P("lat", "lon", None), check_vma=False
    )
```

```python
import math

import jax
import jax.numpy as jnp
from jax import lax
from jax.sharding import PartitionSpec as P


def shifted_from(block, axis, distance):
    count = lax.axis_size(axis)
    route = [(i, (i + distance) % count) for i in range(count)]
    return lax.ppermute(block, axis, route)


def face_flux(far_lo, near_lo, near_hi, far_hi, courant):
    centred = (7.0 * (near_lo + near_hi) - (far_lo + far_hi)) / 12.0
    return courant * centred - 0.5 * jnp.abs(courant) * (near_hi - near_lo)


def build_table(n_full, n_waves):
    points = jnp.arange(n_full, dtype=jnp.int32)
    waves = jnp.arange(n_waves, dtype=jnp.int32)
    phase = points[:, None] * waves[None, :] % n_full
    angle = phase.astype(jnp.float32) * (2.0 * math.pi / n_full)
    return jnp.concatenate([jnp.cos(angle), jnp.sin(angle)], axis=1)


def local(state, courant_east, courant_north, cutoff, filter_mask):
    n_rows, n_cols, n_comp = state.shape
    lon_count = lax.axis_size("lon")
    lat_count = lax.axis_size("lat")
    lat_index = lax.axis_index("lat")
    n_full = n_cols * lon_count
    n_lat = n_rows * lat_count
    half = n_full // 2
    group = n_comp // lon_count
    n_ext = n_rows + 4
    n_win = n_cols + 4

    top = n_full // 8 + (half - 1 - n_full // 8) * (n_lat // 4 - 1) // (n_lat // 2)
    n_waves = min(top, half - 1) + 1

    def row_info(sel):
        whole = jnp.concatenate([cutoff[sel], filter_mask[sel]]).astype(jnp.float32)
        blank = jnp.zeros((1, n_cols, n_comp), jnp.float32)
        return blank.at[0, 0, : whole.shape[0]].set(whole)

    from_south = shifted_from(
        jnp.concatenate(
            [state[-2:], courant_north[-1:], row_info(slice(n_rows - 2, n_rows))], axis=0
        ),
        "lat",
        1,
    )
    from_north = shifted_from(
        jnp.concatenate([state[:2], row_info(slice(0, 2))], axis=0), "lat", -1
    )
    east_halo = shifted_from(courant_east[:, -1:], "lon", 1)

    rows_ext = jnp.concatenate([from_south[:2], state, from_north[:2]], axis=0)
    outgoing = rows_ext.reshape(n_ext * n_cols, n_comp).T.reshape(lon_count, -1)
    incoming = lax.all_to_all(outgoing, "lon", split_axis=0, concat_axis=0, tiled=True)
    lines = incoming.reshape(lon_count, group * n_ext, n_cols)
    lines = jnp.transpose(lines, (1, 0, 2)).reshape(group * n_ext, n_full)

    info_s = from_south[3, 0, :4].astype(jnp.int32)
    info_n = from_north[2, 0, :4].astype(jnp.int32)
    cut_ext = jnp.concatenate([info_s[:2], cutoff, info_n[:2]])
    mask_ext = jnp.concatenate([info_s[2:], filter_mask, info_n[2:]])

    fourier = build_table(n_full, n_waves)
    waves = jnp.arange(n_waves, dtype=jnp.int32)
    weights = jnp.where(waves == 0, 1.0 / n_full, 2.0 / n_full).astype(jnp.float32)
    kept = jnp.where(waves[None, :] <= cut_ext[:, None], weights[None, :], 0.0)
    kept_both = jnp.tile(jnp.concatenate([kept, kept], axis=1), (group, 1))
    coeffs = jnp.dot(lines, fourier, precision=lax.Precision.HIGHEST)
    coeffs = coeffs * kept_both
    filtered = lax.dot_general(
        coeffs, fourier, (((1,), (1,)), ((), ())), precision=lax.Precision.HIGHEST
    )
    keep = jnp.tile(mask_ext, group)[:, None] == 1
    smooth = jnp.where(keep, filtered, lines).reshape(group, n_ext, n_full)

    south_pole = jnp.roll(smooth[:, 3:1:-1], half, axis=2)
    north_pole = jnp.roll(smooth[:, n_ext - 3 : n_ext - 5 : -1], half, axis=2)
    low = jnp.where(lat_index == 0, south_pole, smooth[:, :2])
    high = jnp.where(lat_index == lat_count - 1, north_pole, smooth[:, -2:])
    smooth = jnp.concatenate([low, smooth[:, 2:-2], high], axis=1)

    tiles = smooth.reshape(group, n_ext, lon_count, n_cols)
    left = jnp.roll(tiles[..., -2:], 1, axis=2)
    right = jnp.roll(tiles[..., :2], -1, axis=2)
    windows = jnp.concatenate([left, tiles, right], axis=3)
    windows = jnp.transpose(windows, (2, 0, 1, 3)).reshape(lon_count, -1)
    back = lax.all_to_all(windows, "lon", split_axis=0, concat_axis=0, tiled=True)
    ext = back.reshape(n_comp, n_ext * n_win).T.reshape(n_ext, n_win, n_comp)

    zonal_p = ext[2:-2]
    zonal_c = jnp.concatenate([east_halo, courant_east], axis=1)
    east = face_flux(
        zonal_p[:, 0 : n_cols + 1],
        zonal_p[:, 1 : n_cols + 2],
        zonal_p[:, 2 : n_cols + 3],
        zonal_p[:, 3 : n_cols + 4],
        zonal_c,
    )
    zonal = -(east[:, 1:] - east[:, :-1])

    merid_p = ext[:, 2:-2]
    south_c = jnp.where(lat_index == 0, 0.0, from_south[2:3])
    merid_c = jnp.concatenate([south_c, courant_north], axis=0)
    north_flux = face_flux(
        merid_p[0 : n_rows + 1],
        merid_p[1 : n_rows + 2],
        merid_p[2 : n_rows + 3],
        merid_p[3 : n_rows + 4],
        merid_c,
    )
    face_rows = lat_index * n_rows + jnp.arange(-1, n_rows, dtype=jnp.int32)
    cos_face = jnp.sin(
        jnp.minimum(face_rows + 1, n_lat - 1 - face_rows).astype(jnp.float32) * (math.pi / n_lat)
    )
    cell_rows = face_rows[1:]
    cos_cell = jnp.sin(
        (jnp.minimum(cell_rows, n_lat - 1 - cell_rows).astype(jnp.float32) + 0.5)
        * (math.pi / n_lat)
    )
    weighted = cos_face[:, None, None] * north_flux
    meridional = -(weighted[1:] - weighted[:-1]) / cos_cell[:, None, None]
    return zonal_p[:, 2:-2] + zonal + meridional


def solution(mesh):
    placed = (
        P("lat", "lon", None),
        P("lat", "lon", None),
        P("lat", "lon", None),
        P("lat"),
        P("lat"),
    )
    return jax.shard_map(
        local, mesh=mesh, in_specs=placed, out_specs=P("lat", "lon", None), check_vma=False
    )
```

```python
import math

import jax
import jax.numpy as jnp
from jax import lax
from jax.sharding import PartitionSpec as P


def shifted_from(block, axis, distance, wrap=True):
    count = lax.axis_size(axis)
    route = [(i, (i + distance) % count) for i in range(count)]
    if not wrap:
        route = [(i, j) for i, j in route if 0 <= i + distance < count]
    return lax.ppermute(block, axis, route)


def face_flux(far_lo, near_lo, near_hi, far_hi, courant):
    centred = (7.0 * (near_lo + near_hi) - (far_lo + far_hi)) / 12.0
    return courant * centred - 0.5 * jnp.abs(courant) * (near_hi - near_lo)


def build_table(n_full, n_waves, step):
    waves = jnp.arange(n_waves, dtype=jnp.int32)
    coarse = jnp.arange(n_full // step, dtype=jnp.int32) * step
    fine = jnp.arange(step, dtype=jnp.int32)
    scale = 2.0 * math.pi / n_full
    alpha = (coarse[:, None] * waves[None, :] % n_full).astype(jnp.float32) * scale
    beta = (fine[:, None] * waves[None, :] % n_full).astype(jnp.float32) * scale
    ca, sa = jnp.cos(alpha)[:, None], jnp.sin(alpha)[:, None]
    cb, sb = jnp.cos(beta)[None], jnp.sin(beta)[None]
    cos_t = (ca * cb - sa * sb).reshape(n_full, n_waves)
    sin_t = (sa * cb + ca * sb).reshape(n_full, n_waves)
    return jnp.concatenate([cos_t, sin_t], axis=1)


def local(state, courant_east, courant_north, cutoff, filter_mask):
    n_rows, n_cols, n_comp = state.shape
    lon_count = lax.axis_size("lon")
    lat_count = lax.axis_size("lat")
    lat_index = lax.axis_index("lat")
    n_full = n_cols * lon_count
    n_lat = n_rows * lat_count
    half = n_full // 2
    group = n_comp // lon_count
    n_ext = n_rows + 4
    n_win = n_cols + 4

    top = n_full // 8 + (half - 1 - n_full // 8) * (n_lat // 4 - 1) // (n_lat // 2)
    n_waves = min(top, half - 1) + 1

    def row_info(sel):
        whole = jnp.concatenate([cutoff[sel], filter_mask[sel]]).astype(jnp.float32)
        blank = jnp.zeros((1, n_cols, n_comp), jnp.float32)
        return blank.at[0, 0, : whole.shape[0]].set(whole)

    from_south = shifted_from(
        jnp.concatenate(
            [state[-2:], courant_north[-1:], row_info(slice(n_rows - 2, n_rows))], axis=0
        ),
        "lat",
        1,
        wrap=False,
    )
    from_north = shifted_from(
        jnp.concatenate([state[:2], row_info(slice(0, 2))], axis=0), "lat", -1, wrap=False
    )
    east_halo = shifted_from(courant_east[:, -1:], "lon", 1)

    rows_ext = jnp.concatenate([from_south[:2], state, from_north[:2]], axis=0)
    outgoing = rows_ext.reshape(n_ext * n_cols, n_comp).T.reshape(lon_count, -1)
    incoming = lax.all_to_all(outgoing, "lon", split_axis=0, concat_axis=0, tiled=True)
    lines = incoming.reshape(lon_count, group * n_ext, n_cols)
    lines = jnp.transpose(lines, (1, 0, 2)).reshape(group * n_ext, n_full)

    info_s = from_south[3, 0, :4].astype(jnp.int32)
    info_n = from_north[2, 0, :4].astype(jnp.int32)
    cut_ext = jnp.concatenate([info_s[:2], cutoff, info_n[:2]])
    mask_ext = jnp.concatenate([info_s[2:], filter_mask, info_n[2:]])

    fourier = build_table(n_full, n_waves, 32)
    waves = jnp.arange(n_waves, dtype=jnp.int32)
    weights = jnp.where(waves == 0, 1.0 / n_full, 2.0 / n_full).astype(jnp.float32)
    kept = jnp.where(waves[None, :] <= cut_ext[:, None], weights[None, :], 0.0)
    kept_both = jnp.tile(jnp.concatenate([kept, kept], axis=1), (group, 1))
    coeffs = jnp.dot(lines, fourier, precision=lax.Precision.HIGHEST)
    coeffs = coeffs * kept_both
    filtered = lax.dot_general(
        coeffs, fourier, (((1,), (1,)), ((), ())), precision=lax.Precision.HIGHEST
    )
    keep = jnp.tile(mask_ext, group)[:, None] == 1
    smooth = jnp.where(keep, filtered, lines).reshape(group, n_ext, n_full)

    south_pole = jnp.roll(smooth[:, 3:1:-1], half, axis=2)
    north_pole = jnp.roll(smooth[:, n_ext - 3 : n_ext - 5 : -1], half, axis=2)
    low = jnp.where(lat_index == 0, south_pole, smooth[:, :2])
    high = jnp.where(lat_index == lat_count - 1, north_pole, smooth[:, -2:])
    smooth = jnp.concatenate([low, smooth[:, 2:-2], high], axis=1)

    tiles = smooth.reshape(group, n_ext, lon_count, n_cols)
    left = jnp.roll(tiles[..., -2:], 1, axis=2)
    right = jnp.roll(tiles[..., :2], -1, axis=2)
    windows = jnp.concatenate([left, tiles, right], axis=3)
    windows = jnp.transpose(windows, (2, 0, 1, 3)).reshape(lon_count, -1)
    back = lax.all_to_all(windows, "lon", split_axis=0, concat_axis=0, tiled=True)
    ext = back.reshape(n_comp, n_ext * n_win).T.reshape(n_ext, n_win, n_comp)

    zonal_p = ext[2:-2]
    zonal_c = jnp.concatenate([east_halo, courant_east], axis=1)
    east = face_flux(
        zonal_p[:, 0 : n_cols + 1],
        zonal_p[:, 1 : n_cols + 2],
        zonal_p[:, 2 : n_cols + 3],
        zonal_p[:, 3 : n_cols + 4],
        zonal_c,
    )
    zonal = -(east[:, 1:] - east[:, :-1])

    merid_p = ext[:, 2:-2]
    south_c = jnp.where(lat_index == 0, 0.0, from_south[2:3])
    merid_c = jnp.concatenate([south_c, courant_north], axis=0)
    north_flux = face_flux(
        merid_p[0 : n_rows + 1],
        merid_p[1 : n_rows + 2],
        merid_p[2 : n_rows + 3],
        merid_p[3 : n_rows + 4],
        merid_c,
    )
    face_rows = lat_index * n_rows + jnp.arange(-1, n_rows, dtype=jnp.int32)
    cos_face = jnp.sin(
        jnp.minimum(face_rows + 1, n_lat - 1 - face_rows).astype(jnp.float32) * (math.pi / n_lat)
    )
    cell_rows = face_rows[1:]
    cos_cell = jnp.sin(
        (jnp.minimum(cell_rows, n_lat - 1 - cell_rows).astype(jnp.float32) + 0.5)
        * (math.pi / n_lat)
    )
    weighted = cos_face[:, None, None] * north_flux
    meridional = -(weighted[1:] - weighted[:-1]) / cos_cell[:, None, None]
    return zonal_p[:, 2:-2] + zonal + meridional


def solution(mesh):
    placed = (
        P("lat", "lon", None),
        P("lat", "lon", None),
        P("lat", "lon", None),
        P("lat"),
        P("lat"),
    )
    return jax.shard_map(
        local, mesh=mesh, in_specs=placed, out_specs=P("lat", "lon", None), check_vma=False
    )
```

```python
import math

import jax
import jax.numpy as jnp
from jax import lax
from jax.sharding import PartitionSpec as P


def shifted_from(block, axis, distance, wrap=True):
    count = lax.axis_size(axis)
    route = [(i, (i + distance) % count) for i in range(count)]
    if not wrap:
        route = [(i, j) for i, j in route if 0 <= i + distance < count]
    return lax.ppermute(block, axis, route)


def face_flux(far_lo, near_lo, near_hi, far_hi, courant):
    centred = (7.0 * (near_lo + near_hi) - (far_lo + far_hi)) / 12.0
    return courant * centred - 0.5 * jnp.abs(courant) * (near_hi - near_lo)


def build_table(n_full, n_waves, step):
    waves = jnp.arange(n_waves, dtype=jnp.int32)
    coarse = jnp.arange(n_full // step, dtype=jnp.int32) * step
    fine = jnp.arange(step, dtype=jnp.int32)
    scale = 2.0 * math.pi / n_full
    alpha = (coarse[:, None] * waves[None, :] % n_full).astype(jnp.float32) * scale
    beta = (fine[:, None] * waves[None, :] % n_full).astype(jnp.float32) * scale
    ca, sa = jnp.cos(alpha)[:, None], jnp.sin(alpha)[:, None]
    cb, sb = jnp.cos(beta)[None], jnp.sin(beta)[None]
    cos_t = (ca * cb - sa * sb).reshape(n_full, n_waves)
    sin_t = (sa * cb + ca * sb).reshape(n_full, n_waves)
    return jnp.concatenate([cos_t, sin_t], axis=1)


def local(state, courant_east, courant_north, cutoff, filter_mask):
    n_rows, n_cols, n_comp = state.shape
    lon_count = lax.axis_size("lon")
    lat_count = lax.axis_size("lat")
    lat_index = lax.axis_index("lat")
    n_full = n_cols * lon_count
    n_lat = n_rows * lat_count
    half = n_full // 2
    group = n_comp // lon_count
    n_ext = n_rows + 4
    n_win = n_cols + 4

    top = n_full // 8 + (half - 1 - n_full // 8) * (n_lat // 4 - 1) // (n_lat // 2)
    n_waves = min(top, half - 1) + 1

    def row_info(sel):
        whole = jnp.concatenate([cutoff[sel], filter_mask[sel]]).astype(jnp.float32)
        blank = jnp.zeros((1, n_cols, n_comp), jnp.float32)
        return blank.at[0, 0, : whole.shape[0]].set(whole)

    from_south = shifted_from(
        jnp.concatenate(
            [state[-2:], courant_north[-1:], row_info(slice(n_rows - 2, n_rows))], axis=0
        ),
        "lat",
        1,
        wrap=False,
    )
    from_north = shifted_from(
        jnp.concatenate([state[:2], row_info(slice(0, 2))], axis=0), "lat", -1, wrap=False
    )
    east_halo = shifted_from(courant_east[:, -1:], "lon", 1)

    rows_ext = jnp.concatenate([from_south[:2], state, from_north[:2]], axis=0)
    outgoing = rows_ext.reshape(n_ext * n_cols, n_comp).T.reshape(lon_count, -1)
    incoming = lax.all_to_all(outgoing, "lon", split_axis=0, concat_axis=0, tiled=True)
    lines = incoming.reshape(lon_count, group * n_ext, n_cols)
    lines = jnp.transpose(lines, (1, 0, 2)).reshape(group * n_ext, n_full)

    info_s = from_south[3, 0, :4].astype(jnp.int32)
    info_n = from_north[2, 0, :4].astype(jnp.int32)
    cut_ext = jnp.concatenate([info_s[:2], cutoff, info_n[:2]])
    mask_ext = jnp.concatenate([info_s[2:], filter_mask, info_n[2:]])

    fourier = build_table(n_full, n_waves, 32)
    waves = jnp.arange(n_waves, dtype=jnp.int32)
    weights = jnp.where(waves == 0, 1.0 / n_full, 2.0 / n_full).astype(jnp.float32)
    kept = jnp.where(waves[None, :] <= cut_ext[:, None], weights[None, :], 0.0)
    kept_both = jnp.tile(jnp.concatenate([kept, kept], axis=1), (group, 1))
    coeffs = jnp.dot(lines, fourier, precision=lax.Precision.HIGH)
    coeffs = coeffs * kept_both
    filtered = lax.dot_general(
        coeffs, fourier, (((1,), (1,)), ((), ())), precision=lax.Precision.HIGH
    )
    keep = jnp.tile(mask_ext, group)[:, None] == 1
    smooth = jnp.where(keep, filtered, lines).reshape(group, n_ext, n_full)

    south_pole = jnp.roll(smooth[:, 3:1:-1], half, axis=2)
    north_pole = jnp.roll(smooth[:, n_ext - 3 : n_ext - 5 : -1], half, axis=2)
    low = jnp.where(lat_index == 0, south_pole, smooth[:, :2])
    high = jnp.where(lat_index == lat_count - 1, north_pole, smooth[:, -2:])
    smooth = jnp.concatenate([low, smooth[:, 2:-2], high], axis=1)

    tiles = smooth.reshape(group, n_ext, lon_count, n_cols)
    left = jnp.roll(tiles[..., -2:], 1, axis=2)
    right = jnp.roll(tiles[..., :2], -1, axis=2)
    windows = jnp.concatenate([left, tiles, right], axis=3)
    windows = jnp.transpose(windows, (2, 0, 1, 3)).reshape(lon_count, -1)
    back = lax.all_to_all(windows, "lon", split_axis=0, concat_axis=0, tiled=True)
    ext = back.reshape(n_comp, n_ext * n_win).T.reshape(n_ext, n_win, n_comp)

    zonal_p = ext[2:-2]
    zonal_c = jnp.concatenate([east_halo, courant_east], axis=1)
    east = face_flux(
        zonal_p[:, 0 : n_cols + 1],
        zonal_p[:, 1 : n_cols + 2],
        zonal_p[:, 2 : n_cols + 3],
        zonal_p[:, 3 : n_cols + 4],
        zonal_c,
    )
    zonal = -(east[:, 1:] - east[:, :-1])

    merid_p = ext[:, 2:-2]
    south_c = jnp.where(lat_index == 0, 0.0, from_south[2:3])
    merid_c = jnp.concatenate([south_c, courant_north], axis=0)
    north_flux = face_flux(
        merid_p[0 : n_rows + 1],
        merid_p[1 : n_rows + 2],
        merid_p[2 : n_rows + 3],
        merid_p[3 : n_rows + 4],
        merid_c,
    )
    face_rows = lat_index * n_rows + jnp.arange(-1, n_rows, dtype=jnp.int32)
    cos_face = jnp.sin(
        jnp.minimum(face_rows + 1, n_lat - 1 - face_rows).astype(jnp.float32) * (math.pi / n_lat)
    )
    cell_rows = face_rows[1:]
    cos_cell = jnp.sin(
        (jnp.minimum(cell_rows, n_lat - 1 - cell_rows).astype(jnp.float32) + 0.5)
        * (math.pi / n_lat)
    )
    weighted = cos_face[:, None, None] * north_flux
    meridional = -(weighted[1:] - weighted[:-1]) / cos_cell[:, None, None]
    return zonal_p[:, 2:-2] + zonal + meridional


def solution(mesh):
    placed = (
        P("lat", "lon", None),
        P("lat", "lon", None),
        P("lat", "lon", None),
        P("lat"),
        P("lat"),
    )
    return jax.shard_map(
        local, mesh=mesh, in_specs=placed, out_specs=P("lat", "lon", None), check_vma=False
    )
```

```python
import math

import jax
import jax.numpy as jnp
from jax import lax
from jax.sharding import PartitionSpec as P


def shifted_from(block, axis, distance, wrap=True):
    count = lax.axis_size(axis)
    route = [(i, (i + distance) % count) for i in range(count)]
    if not wrap:
        route = [(i, j) for i, j in route if 0 <= i + distance < count]
    return lax.ppermute(block, axis, route)


def face_flux(far_lo, near_lo, near_hi, far_hi, courant):
    centred = (7.0 * (near_lo + near_hi) - (far_lo + far_hi)) / 12.0
    return courant * centred - 0.5 * jnp.abs(courant) * (near_hi - near_lo)


def build_table(n_full, n_waves, step):
    waves = jnp.arange(n_waves, dtype=jnp.int32)
    coarse = jnp.arange(n_full // step, dtype=jnp.int32) * step
    fine = jnp.arange(step, dtype=jnp.int32)
    scale = 2.0 * math.pi / n_full
    alpha = (coarse[:, None] * waves[None, :] % n_full).astype(jnp.float32) * scale
    beta = (fine[:, None] * waves[None, :] % n_full).astype(jnp.float32) * scale
    ca, sa = jnp.cos(alpha)[:, None], jnp.sin(alpha)[:, None]
    cb, sb = jnp.cos(beta)[None], jnp.sin(beta)[None]
    cos_t = (ca * cb - sa * sb).reshape(n_full, n_waves)
    sin_t = (sa * cb + ca * sb).reshape(n_full, n_waves)
    return jnp.concatenate([cos_t, sin_t], axis=1)


def local(state, courant_east, courant_north, cutoff, filter_mask):
    n_rows, n_cols, n_comp = state.shape
    lon_count = lax.axis_size("lon")
    lat_count = lax.axis_size("lat")
    lat_index = lax.axis_index("lat")
    n_full = n_cols * lon_count
    n_lat = n_rows * lat_count
    half = n_full // 2
    group = n_comp // lon_count
    n_send = n_rows + 2
    n_win = n_cols + 4

    top = n_full // 8 + (half - 1 - n_full // 8) * (n_lat // 4 - 1) // (n_lat // 2)
    n_waves = min(top, half - 1) + 1

    east_halo = shifted_from(courant_east[:, -1:], "lon", 1)

    outgoing = state.reshape(n_rows * n_cols, n_comp).T.reshape(lon_count, -1)
    incoming = lax.all_to_all(outgoing, "lon", split_axis=0, concat_axis=0, tiled=True)
    lines = incoming.reshape(lon_count, group * n_rows, n_cols)
    lines = jnp.transpose(lines, (1, 0, 2)).reshape(group * n_rows, n_full)

    fourier = build_table(n_full, n_waves, 32)
    waves = jnp.arange(n_waves, dtype=jnp.int32)
    weights = jnp.where(waves == 0, 1.0 / n_full, 2.0 / n_full).astype(jnp.float32)
    kept = jnp.where(waves[None, :] <= cutoff[:, None], weights[None, :], 0.0)
    kept_both = jnp.tile(jnp.concatenate([kept, kept], axis=1), (group, 1))
    coeffs = jnp.dot(lines, fourier, precision=lax.Precision.HIGH)
    coeffs = coeffs * kept_both
    filtered = lax.dot_general(
        coeffs, fourier, (((1,), (1,)), ((), ())), precision=lax.Precision.HIGH
    )
    keep = jnp.tile(filter_mask, group)[:, None] == 1
    smooth = jnp.where(keep, filtered, lines).reshape(group, n_rows, n_full)

    south_pole = smooth[:, 1::-1]
    north_pole = smooth[:, : n_rows - 3 : -1]
    pole = jnp.roll(jnp.where(lat_index == 0, south_pole, north_pole), half, axis=2)
    rows_out = jnp.concatenate([pole, smooth], axis=1)

    tiles = rows_out.reshape(group, n_send, lon_count, n_cols)
    left = jnp.roll(tiles[..., -2:], 1, axis=2)
    right = jnp.roll(tiles[..., :2], -1, axis=2)
    windows = jnp.concatenate([left, tiles, right], axis=3)
    windows = jnp.transpose(windows, (2, 0, 1, 3)).reshape(lon_count, -1)
    back = lax.all_to_all(windows, "lon", split_axis=0, concat_axis=0, tiled=True)
    ext = back.reshape(n_comp, n_send * n_win).T.reshape(n_send, n_win, n_comp)
    own = ext[2:]
    centre = own[:, 2:-2]

    from_south = shifted_from(
        jnp.concatenate([centre[-2:], courant_north[-1:]], axis=0), "lat", 1, wrap=False
    )
    from_north = shifted_from(centre[:2], "lat", -1, wrap=False)

    zonal_c = jnp.concatenate([east_halo, courant_east], axis=1)
    east = face_flux(
        own[:, 0 : n_cols + 1],
        own[:, 1 : n_cols + 2],
        own[:, 2 : n_cols + 3],
        own[:, 3 : n_cols + 4],
        zonal_c,
    )
    zonal = -(east[:, 1:] - east[:, :-1])

    pole_rows = ext[:2, 2:-2]
    south = jnp.where(lat_index == 0, pole_rows, from_south[:2])
    north = jnp.where(lat_index == lat_count - 1, pole_rows, from_north)
    merid_p = jnp.concatenate([south, centre, north], axis=0)
    south_c = jnp.where(lat_index == 0, 0.0, from_south[2:3])
    merid_c = jnp.concatenate([south_c, courant_north], axis=0)
    north_flux = face_flux(
        merid_p[0 : n_rows + 1],
        merid_p[1 : n_rows + 2],
        merid_p[2 : n_rows + 3],
        merid_p[3 : n_rows + 4],
        merid_c,
    )
    face_rows = lat_index * n_rows + jnp.arange(-1, n_rows, dtype=jnp.int32)
    cos_face = jnp.sin(
        jnp.minimum(face_rows + 1, n_lat - 1 - face_rows).astype(jnp.float32) * (math.pi / n_lat)
    )
    cell_rows = face_rows[1:]
    cos_cell = jnp.sin(
        (jnp.minimum(cell_rows, n_lat - 1 - cell_rows).astype(jnp.float32) + 0.5)
        * (math.pi / n_lat)
    )
    weighted = cos_face[:, None, None] * north_flux
    meridional = -(weighted[1:] - weighted[:-1]) / cos_cell[:, None, None]
    return centre + zonal + meridional


def solution(mesh):
    placed = (
        P("lat", "lon", None),
        P("lat", "lon", None),
        P("lat", "lon", None),
        P("lat"),
        P("lat"),
    )
    return jax.shard_map(
        local, mesh=mesh, in_specs=placed, out_specs=P("lat", "lon", None), check_vma=False
    )
```

```python
import math

import jax
import jax.numpy as jnp
from jax import lax
from jax.sharding import PartitionSpec as P


def shifted_from(block, axis, distance, wrap=True):
    count = lax.axis_size(axis)
    route = [(i, (i + distance) % count) for i in range(count)]
    if not wrap:
        route = [(i, j) for i, j in route if 0 <= i + distance < count]
    return lax.ppermute(block, axis, route)


def face_flux(far_lo, near_lo, near_hi, far_hi, courant):
    centred = (7.0 * (near_lo + near_hi) - (far_lo + far_hi)) / 12.0
    return courant * centred - 0.5 * jnp.abs(courant) * (near_hi - near_lo)


def build_table(n_full, n_waves, step):
    waves = jnp.arange(n_waves, dtype=jnp.int32)
    coarse = jnp.arange(n_full // step, dtype=jnp.int32) * step
    fine = jnp.arange(step, dtype=jnp.int32)
    scale = 2.0 * math.pi / n_full
    alpha = (coarse[:, None] * waves[None, :] % n_full).astype(jnp.float32) * scale
    beta = (fine[:, None] * waves[None, :] % n_full).astype(jnp.float32) * scale
    ca, sa = jnp.cos(alpha)[:, None], jnp.sin(alpha)[:, None]
    cb, sb = jnp.cos(beta)[None], jnp.sin(beta)[None]
    cos_t = (ca * cb - sa * sb).reshape(n_full, n_waves)
    sin_t = (sa * cb + ca * sb).reshape(n_full, n_waves)
    return jnp.concatenate([cos_t, sin_t], axis=1)


def local(state, courant_east, courant_north, cutoff, filter_mask):
    n_rows, n_cols, n_comp = state.shape
    lon_count = lax.axis_size("lon")
    lat_count = lax.axis_size("lat")
    lat_index = lax.axis_index("lat")
    n_full = n_cols * lon_count
    n_lat = n_rows * lat_count
    half = n_full // 2
    group = n_comp // lon_count
    n_send = n_rows + 2
    n_win = n_cols + 4

    top = n_full // 8 + (half - 1 - n_full // 8) * (n_lat // 4 - 1) // (n_lat // 2)
    n_waves = min(top, half - 1) + 1

    east_halo = shifted_from(courant_east[:, -1:], "lon", 1)

    def through_filter(state, cutoff, filter_mask):
        outgoing = state.reshape(n_rows * n_cols, n_comp).T.reshape(lon_count, -1)
        incoming = lax.all_to_all(outgoing, "lon", split_axis=0, concat_axis=0, tiled=True)
        lines = incoming.reshape(lon_count, group * n_rows, n_cols)
        lines = jnp.transpose(lines, (1, 0, 2)).reshape(group * n_rows, n_full)

        fourier = build_table(n_full, n_waves, 32)
        waves = jnp.arange(n_waves, dtype=jnp.int32)
        weights = jnp.where(waves == 0, 1.0 / n_full, 2.0 / n_full).astype(jnp.float32)
        kept = jnp.where(waves[None, :] <= cutoff[:, None], weights[None, :], 0.0)
        kept_both = jnp.tile(jnp.concatenate([kept, kept], axis=1), (group, 1))
        coeffs = jnp.dot(lines, fourier, precision=lax.Precision.HIGH)
        coeffs = coeffs * kept_both
        filtered = lax.dot_general(
            coeffs, fourier, (((1,), (1,)), ((), ())), precision=lax.Precision.HIGH
        )
        keep = jnp.tile(filter_mask, group)[:, None] == 1
        smooth = jnp.where(keep, filtered, lines).reshape(group, n_rows, n_full)

        south_pole = smooth[:, 1::-1]
        north_pole = smooth[:, : n_rows - 3 : -1]
        pole = jnp.roll(jnp.where(lat_index == 0, south_pole, north_pole), half, axis=2)
        rows_out = jnp.concatenate([pole, smooth], axis=1)

        tiles = rows_out.reshape(group, n_send, lon_count, n_cols)
        left = jnp.roll(tiles[..., -2:], 1, axis=2)
        right = jnp.roll(tiles[..., :2], -1, axis=2)
        windows = jnp.concatenate([left, tiles, right], axis=3)
        windows = jnp.transpose(windows, (2, 0, 1, 3)).reshape(lon_count, -1)
        back = lax.all_to_all(windows, "lon", split_axis=0, concat_axis=0, tiled=True)
        ext = back.reshape(n_comp, n_send * n_win).T.reshape(n_send, n_win, n_comp)
        return ext

    def as_state(state, cutoff, filter_mask):
        from_west = shifted_from(state[:, -2:], "lon", 1)
        from_east = shifted_from(state[:, :2], "lon", -1)
        rows = jnp.concatenate([from_west, state, from_east], axis=1)
        return jnp.concatenate([jnp.zeros_like(rows[:2]), rows], axis=0)

    reach = n_lat // 4
    first = lat_index * n_rows
    plain = (first >= reach) & (first + n_rows - 1 <= n_lat - 1 - reach)
    ext = lax.cond(plain, as_state, through_filter, state, cutoff, filter_mask)
    own = ext[2:]
    centre = own[:, 2:-2]

    from_south = shifted_from(
        jnp.concatenate([centre[-2:], courant_north[-1:]], axis=0), "lat", 1, wrap=False
    )
    from_north = shifted_from(centre[:2], "lat", -1, wrap=False)

    zonal_c = jnp.concatenate([east_halo, courant_east], axis=1)
    east = face_flux(
        own[:, 0 : n_cols + 1],
        own[:, 1 : n_cols + 2],
        own[:, 2 : n_cols + 3],
        own[:, 3 : n_cols + 4],
        zonal_c,
    )
    zonal = -(east[:, 1:] - east[:, :-1])

    pole_rows = ext[:2, 2:-2]
    south = jnp.where(lat_index == 0, pole_rows, from_south[:2])
    north = jnp.where(lat_index == lat_count - 1, pole_rows, from_north)
    merid_p = jnp.concatenate([south, centre, north], axis=0)
    south_c = jnp.where(lat_index == 0, 0.0, from_south[2:3])
    merid_c = jnp.concatenate([south_c, courant_north], axis=0)
    north_flux = face_flux(
        merid_p[0 : n_rows + 1],
        merid_p[1 : n_rows + 2],
        merid_p[2 : n_rows + 3],
        merid_p[3 : n_rows + 4],
        merid_c,
    )
    face_rows = lat_index * n_rows + jnp.arange(-1, n_rows, dtype=jnp.int32)
    cos_face = jnp.sin(
        jnp.minimum(face_rows + 1, n_lat - 1 - face_rows).astype(jnp.float32) * (math.pi / n_lat)
    )
    cell_rows = face_rows[1:]
    cos_cell = jnp.sin(
        (jnp.minimum(cell_rows, n_lat - 1 - cell_rows).astype(jnp.float32) + 0.5)
        * (math.pi / n_lat)
    )
    weighted = cos_face[:, None, None] * north_flux
    meridional = -(weighted[1:] - weighted[:-1]) / cos_cell[:, None, None]
    return centre + zonal + meridional


def solution(mesh):
    placed = (
        P("lat", "lon", None),
        P("lat", "lon", None),
        P("lat", "lon", None),
        P("lat"),
        P("lat"),
    )
    return jax.shard_map(
        local, mesh=mesh, in_specs=placed, out_specs=P("lat", "lon", None), check_vma=False
    )
```

```python
import math

import jax
import jax.numpy as jnp
from jax import lax
from jax.sharding import PartitionSpec as P


def shifted_from(block, axis, distance, wrap=True):
    count = lax.axis_size(axis)
    route = [(i, (i + distance) % count) for i in range(count)]
    if not wrap:
        route = [(i, j) for i, j in route if 0 <= i + distance < count]
    return lax.ppermute(block, axis, route)


def face_flux(far_lo, near_lo, near_hi, far_hi, courant):
    centred = (7.0 * (near_lo + near_hi) - (far_lo + far_hi)) / 12.0
    return courant * centred - 0.5 * jnp.abs(courant) * (near_hi - near_lo)


def build_table(n_full, n_waves, step):
    waves = jnp.arange(n_waves, dtype=jnp.int32)
    coarse = jnp.arange(n_full // step, dtype=jnp.int32) * step
    fine = jnp.arange(step, dtype=jnp.int32)
    scale = 2.0 * math.pi / n_full
    alpha = (coarse[:, None] * waves[None, :] % n_full).astype(jnp.float32) * scale
    beta = (fine[:, None] * waves[None, :] % n_full).astype(jnp.float32) * scale
    ca, sa = jnp.cos(alpha)[:, None], jnp.sin(alpha)[:, None]
    cb, sb = jnp.cos(beta)[None], jnp.sin(beta)[None]
    cos_t = (ca * cb - sa * sb).reshape(n_full, n_waves)
    sin_t = (sa * cb + ca * sb).reshape(n_full, n_waves)
    return jnp.concatenate([cos_t, sin_t], axis=1)


def local(state, courant_east, courant_north, cutoff, filter_mask):
    n_rows, n_cols, n_comp = state.shape
    lon_count = lax.axis_size("lon")
    lat_count = lax.axis_size("lat")
    lat_index = lax.axis_index("lat")
    n_full = n_cols * lon_count
    n_lat = n_rows * lat_count
    half = n_full // 2
    group = n_comp // lon_count
    n_send = n_rows + 2
    n_win = n_cols + 4

    top = n_full // 8 + (half - 1 - n_full // 8) * (n_lat // 4 - 1) // (n_lat // 2)
    n_waves = min(top, half - 1) + 1

    east_halo = shifted_from(courant_east[:, -1:], "lon", 1)

    outgoing = state.reshape(n_rows * n_cols, n_comp).T.reshape(lon_count, -1)
    incoming = lax.all_to_all(outgoing, "lon", split_axis=0, concat_axis=0, tiled=True)
    blocks = incoming.reshape(lon_count, group * n_rows, n_cols)

    fourier = build_table(n_full, n_waves, 32)
    waves = jnp.arange(n_waves, dtype=jnp.int32)
    weights = jnp.where(waves == 0, 1.0 / n_full, 2.0 / n_full).astype(jnp.float32)
    kept = jnp.where(waves[None, :] <= cutoff[:, None], weights[None, :], 0.0)
    kept_both = jnp.tile(jnp.concatenate([kept, kept], axis=1), (group, 1))
    coeffs = lax.dot_general(
        blocks,
        fourier.reshape(lon_count, n_cols, -1),
        (((0, 2), (0, 1)), ((), ())),
        precision=lax.Precision.HIGH,
    )
    coeffs = coeffs * kept_both
    filtered = lax.dot_general(
        coeffs,
        fourier.reshape(lon_count, n_cols, -1),
        (((1,), (2,)), ((), ())),
        precision=lax.Precision.HIGH,
    )
    keep = jnp.tile(filter_mask, group)[:, None, None] == 1
    smooth = jnp.where(keep, filtered, jnp.transpose(blocks, (1, 0, 2)))
    smooth = smooth.reshape(group, n_rows, n_full)

    south_pole = smooth[:, 1::-1]
    north_pole = smooth[:, : n_rows - 3 : -1]
    pole = jnp.roll(jnp.where(lat_index == 0, south_pole, north_pole), half, axis=2)
    rows_out = jnp.concatenate([pole, smooth], axis=1)

    tiles = rows_out.reshape(group, n_send, lon_count, n_cols)
    left = jnp.roll(tiles[..., -2:], 1, axis=2)
    right = jnp.roll(tiles[..., :2], -1, axis=2)
    windows = jnp.concatenate([left, tiles, right], axis=3)
    windows = jnp.transpose(windows, (2, 0, 1, 3)).reshape(lon_count, -1)
    back = lax.all_to_all(windows, "lon", split_axis=0, concat_axis=0, tiled=True)
    ext = back.reshape(n_comp, n_send * n_win).T.reshape(n_send, n_win, n_comp)
    own = ext[2:]
    centre = own[:, 2:-2]

    from_south = shifted_from(
        jnp.concatenate([centre[-2:], courant_north[-1:]], axis=0), "lat", 1, wrap=False
    )
    from_north = shifted_from(centre[:2], "lat", -1, wrap=False)

    zonal_c = jnp.concatenate([east_halo, courant_east], axis=1)
    east = face_flux(
        own[:, 0 : n_cols + 1],
        own[:, 1 : n_cols + 2],
        own[:, 2 : n_cols + 3],
        own[:, 3 : n_cols + 4],
        zonal_c,
    )
    zonal = -(east[:, 1:] - east[:, :-1])

    pole_rows = ext[:2, 2:-2]
    south = jnp.where(lat_index == 0, pole_rows, from_south[:2])
    north = jnp.where(lat_index == lat_count - 1, pole_rows, from_north)
    merid_p = jnp.concatenate([south, centre, north], axis=0)
    south_c = jnp.where(lat_index == 0, 0.0, from_south[2:3])
    merid_c = jnp.concatenate([south_c, courant_north], axis=0)
    north_flux = face_flux(
        merid_p[0 : n_rows + 1],
        merid_p[1 : n_rows + 2],
        merid_p[2 : n_rows + 3],
        merid_p[3 : n_rows + 4],
        merid_c,
    )
    face_rows = lat_index * n_rows + jnp.arange(-1, n_rows, dtype=jnp.int32)
    cos_face = jnp.sin(
        jnp.minimum(face_rows + 1, n_lat - 1 - face_rows).astype(jnp.float32) * (math.pi / n_lat)
    )
    cell_rows = face_rows[1:]
    cos_cell = jnp.sin(
        (jnp.minimum(cell_rows, n_lat - 1 - cell_rows).astype(jnp.float32) + 0.5)
        * (math.pi / n_lat)
    )
    weighted = cos_face[:, None, None] * north_flux
    meridional = -(weighted[1:] - weighted[:-1]) / cos_cell[:, None, None]
    return centre + zonal + meridional


def solution(mesh):
    placed = (
        P("lat", "lon", None),
        P("lat", "lon", None),
        P("lat", "lon", None),
        P("lat"),
        P("lat"),
    )
    return jax.shard_map(
        local, mesh=mesh, in_specs=placed, out_specs=P("lat", "lon", None), check_vma=False
    )
```

```python
import math

import jax
import jax.numpy as jnp
from jax import lax
from jax.sharding import PartitionSpec as P


def shifted_from(block, axis, distance, wrap=True):
    count = lax.axis_size(axis)
    route = [(i, (i + distance) % count) for i in range(count)]
    if not wrap:
        route = [(i, j) for i, j in route if 0 <= i + distance < count]
    return lax.ppermute(block, axis, route)


def face_flux(far_lo, near_lo, near_hi, far_hi, courant):
    centred = (7.0 * (near_lo + near_hi) - (far_lo + far_hi)) / 12.0
    return courant * centred - 0.5 * jnp.abs(courant) * (near_hi - near_lo)


def build_table(n_full, n_waves, step):
    waves = jnp.arange(n_waves, dtype=jnp.int32)
    coarse = jnp.arange(n_full // step, dtype=jnp.int32) * step
    fine = jnp.arange(step, dtype=jnp.int32)
    scale = 2.0 * math.pi / n_full
    alpha = (coarse[:, None] * waves[None, :] % n_full).astype(jnp.float32) * scale
    beta = (fine[:, None] * waves[None, :] % n_full).astype(jnp.float32) * scale
    ca, sa = jnp.cos(alpha)[:, None], jnp.sin(alpha)[:, None]
    cb, sb = jnp.cos(beta)[None], jnp.sin(beta)[None]
    cos_t = (ca * cb - sa * sb).reshape(n_full, n_waves)
    sin_t = (sa * cb + ca * sb).reshape(n_full, n_waves)
    return jnp.concatenate([cos_t, sin_t], axis=1)


def local(state, courant_east, courant_north, cutoff, filter_mask):
    n_rows, n_cols, n_comp = state.shape
    lon_count = lax.axis_size("lon")
    lat_count = lax.axis_size("lat")
    lat_index = lax.axis_index("lat")
    n_full = n_cols * lon_count
    n_lat = n_rows * lat_count
    half = n_full // 2
    group = n_comp // lon_count
    n_send = n_rows + 4
    n_win = n_cols + 4

    top = n_full // 8 + (half - 1 - n_full // 8) * (n_lat // 4 - 1) // (n_lat // 2)
    n_waves = min(top, half - 1) + 1

    east_halo = shifted_from(courant_east[:, -1:], "lon", 1)
    north_halo = shifted_from(courant_north[-1:], "lat", 1, wrap=False)

    outgoing = state.reshape(n_rows * n_cols, n_comp).T.reshape(lon_count, -1)
    incoming = lax.all_to_all(outgoing, "lon", split_axis=0, concat_axis=0, tiled=True)
    blocks = incoming.reshape(lon_count, group * n_rows, n_cols)

    fourier = build_table(n_full, n_waves, 32)
    waves = jnp.arange(n_waves, dtype=jnp.int32)
    weights = jnp.where(waves == 0, 1.0 / n_full, 2.0 / n_full).astype(jnp.float32)
    kept = jnp.where(waves[None, :] <= cutoff[:, None], weights[None, :], 0.0)
    kept_both = jnp.tile(jnp.concatenate([kept, kept], axis=1), (group, 1))
    coeffs = lax.dot_general(
        blocks,
        fourier.reshape(lon_count, n_cols, -1),
        (((0, 2), (0, 1)), ((), ())),
        precision=lax.Precision.HIGH,
    )
    coeffs = coeffs * kept_both
    filtered = lax.dot_general(
        coeffs,
        fourier.reshape(lon_count, n_cols, -1),
        (((1,), (2,)), ((), ())),
        precision=lax.Precision.HIGH,
    )
    keep = jnp.tile(filter_mask, group)[:, None, None] == 1
    smooth = jnp.where(keep, filtered, jnp.transpose(blocks, (1, 0, 2)))
    smooth = smooth.reshape(group, n_rows, n_full)

    from_south = shifted_from(smooth[:, -2:], "lat", 1, wrap=False)
    from_north = shifted_from(smooth[:, :2], "lat", -1, wrap=False)
    south_pole = jnp.roll(smooth[:, 1::-1], half, axis=2)
    north_pole = jnp.roll(smooth[:, : n_rows - 3 : -1], half, axis=2)
    low = jnp.where(lat_index == 0, south_pole, from_south)
    high = jnp.where(lat_index == lat_count - 1, north_pole, from_north)
    rows_out = jnp.concatenate([low, smooth, high], axis=1)

    tiles = rows_out.reshape(group, n_send, lon_count, n_cols)
    left = jnp.roll(tiles[..., -2:], 1, axis=2)
    right = jnp.roll(tiles[..., :2], -1, axis=2)
    windows = jnp.concatenate([left, tiles, right], axis=3)
    windows = jnp.transpose(windows, (2, 0, 1, 3)).reshape(lon_count, -1)
    back = lax.all_to_all(windows, "lon", split_axis=0, concat_axis=0, tiled=True)
    ext = back.reshape(n_comp, n_send * n_win).T.reshape(n_send, n_win, n_comp)
    own = ext[2:-2]
    centre = own[:, 2:-2]

    zonal_c = jnp.concatenate([east_halo, courant_east], axis=1)
    east = face_flux(
        own[:, 0 : n_cols + 1],
        own[:, 1 : n_cols + 2],
        own[:, 2 : n_cols + 3],
        own[:, 3 : n_cols + 4],
        zonal_c,
    )
    zonal = -(east[:, 1:] - east[:, :-1])

    merid_p = ext[:, 2:-2]
    south_c = jnp.where(lat_index == 0, 0.0, north_halo)
    merid_c = jnp.concatenate([south_c, courant_north], axis=0)
    north_flux = face_flux(
        merid_p[0 : n_rows + 1],
        merid_p[1 : n_rows + 2],
        merid_p[2 : n_rows + 3],
        merid_p[3 : n_rows + 4],
        merid_c,
    )
    face_rows = lat_index * n_rows + jnp.arange(-1, n_rows, dtype=jnp.int32)
    cos_face = jnp.sin(
        jnp.minimum(face_rows + 1, n_lat - 1 - face_rows).astype(jnp.float32) * (math.pi / n_lat)
    )
    cell_rows = face_rows[1:]
    cos_cell = jnp.sin(
        (jnp.minimum(cell_rows, n_lat - 1 - cell_rows).astype(jnp.float32) + 0.5)
        * (math.pi / n_lat)
    )
    weighted = cos_face[:, None, None] * north_flux
    meridional = -(weighted[1:] - weighted[:-1]) / cos_cell[:, None, None]
    return centre + zonal + meridional


def solution(mesh):
    placed = (
        P("lat", "lon", None),
        P("lat", "lon", None),
        P("lat", "lon", None),
        P("lat"),
        P("lat"),
    )
    return jax.shard_map(
        local, mesh=mesh, in_specs=placed, out_specs=P("lat", "lon", None), check_vma=False
    )
```

```python
import math

import jax
import jax.numpy as jnp
from jax import lax
from jax.sharding import PartitionSpec as P


def shifted_from(block, axis, distance, wrap=True):
    count = lax.axis_size(axis)
    route = [(i, (i + distance) % count) for i in range(count)]
    if not wrap:
        route = [(i, j) for i, j in route if 0 <= i + distance < count]
    return lax.ppermute(block, axis, route)


def face_flux(far_lo, near_lo, near_hi, far_hi, courant):
    centred = (7.0 * (near_lo + near_hi) - (far_lo + far_hi)) / 12.0
    return courant * centred - 0.5 * jnp.abs(courant) * (near_hi - near_lo)


def build_table(n_full, n_waves, step):
    waves = jnp.arange(n_waves, dtype=jnp.int32)
    coarse = jnp.arange(n_full // step, dtype=jnp.int32) * step
    fine = jnp.arange(step, dtype=jnp.int32)
    scale = 2.0 * math.pi / n_full
    alpha = (coarse[:, None] * waves[None, :] % n_full).astype(jnp.float32) * scale
    beta = (fine[:, None] * waves[None, :] % n_full).astype(jnp.float32) * scale
    ca, sa = jnp.cos(alpha)[:, None], jnp.sin(alpha)[:, None]
    cb, sb = jnp.cos(beta)[None], jnp.sin(beta)[None]
    cos_t = (ca * cb - sa * sb).reshape(n_full, n_waves)
    sin_t = (sa * cb + ca * sb).reshape(n_full, n_waves)
    return jnp.concatenate([cos_t, sin_t], axis=1)


def local(state, courant_east, courant_north, cutoff, filter_mask):
    n_rows, n_cols, n_comp = state.shape
    lon_count = lax.axis_size("lon")
    lat_count = lax.axis_size("lat")
    lat_index = lax.axis_index("lat")
    n_full = n_cols * lon_count
    n_lat = n_rows * lat_count
    half = n_full // 2
    group = n_comp // lon_count
    n_send = n_rows + 4
    n_win = n_cols + 4

    top = n_full // 8 + (half - 1 - n_full // 8) * (n_lat // 4 - 1) // (n_lat // 2)
    n_waves = min(top, half - 1) + 1

    east_halo = shifted_from(courant_east[:, -1:], "lon", 1)
    north_halo = shifted_from(courant_north[-1:], "lat", 1, wrap=False)

    outgoing = state.reshape(n_rows * n_cols, n_comp).T.reshape(lon_count, -1)
    incoming = lax.all_to_all(outgoing, "lon", split_axis=0, concat_axis=0, tiled=True)
    blocks = incoming.reshape(lon_count, group * n_rows, n_cols)
    blocks, east_halo, north_halo = lax.optimization_barrier((blocks, east_halo, north_halo))

    fourier = build_table(n_full, n_waves, 32)
    waves = jnp.arange(n_waves, dtype=jnp.int32)
    weights = jnp.where(waves == 0, 1.0 / n_full, 2.0 / n_full).astype(jnp.float32)
    kept = jnp.where(waves[None, :] <= cutoff[:, None], weights[None, :], 0.0)
    kept_both = jnp.tile(jnp.concatenate([kept, kept], axis=1), (group, 1))
    coeffs = lax.dot_general(
        blocks,
        fourier.reshape(lon_count, n_cols, -1),
        (((0, 2), (0, 1)), ((), ())),
        precision=lax.Precision.HIGH,
    )
    coeffs = coeffs * kept_both
    filtered = lax.dot_general(
        coeffs,
        fourier.reshape(lon_count, n_cols, -1),
        (((1,), (2,)), ((), ())),
        precision=lax.Precision.HIGH,
    )
    keep = jnp.tile(filter_mask, group)[:, None, None] == 1
    smooth = jnp.where(keep, filtered, jnp.transpose(blocks, (1, 0, 2)))
    smooth = smooth.reshape(group, n_rows, n_full)

    from_south = shifted_from(smooth[:, -2:], "lat", 1, wrap=False)
    from_north = shifted_from(smooth[:, :2], "lat", -1, wrap=False)
    south_pole = jnp.roll(smooth[:, 1::-1], half, axis=2)
    north_pole = jnp.roll(smooth[:, : n_rows - 3 : -1], half, axis=2)
    low = jnp.where(lat_index == 0, south_pole, from_south)
    high = jnp.where(lat_index == lat_count - 1, north_pole, from_north)
    rows_out = jnp.concatenate([low, smooth, high], axis=1)

    tiles = rows_out.reshape(group, n_send, lon_count, n_cols)
    left = jnp.roll(tiles[..., -2:], 1, axis=2)
    right = jnp.roll(tiles[..., :2], -1, axis=2)
    windows = jnp.concatenate([left, tiles, right], axis=3)
    windows = jnp.transpose(windows, (2, 0, 1, 3)).reshape(lon_count, -1)
    back = lax.all_to_all(windows, "lon", split_axis=0, concat_axis=0, tiled=True)
    ext = back.reshape(n_comp, n_send * n_win).T.reshape(n_send, n_win, n_comp)
    own = ext[2:-2]
    centre = own[:, 2:-2]

    zonal_c = jnp.concatenate([east_halo, courant_east], axis=1)
    east = face_flux(
        own[:, 0 : n_cols + 1],
        own[:, 1 : n_cols + 2],
        own[:, 2 : n_cols + 3],
        own[:, 3 : n_cols + 4],
        zonal_c,
    )
    zonal = -(east[:, 1:] - east[:, :-1])

    merid_p = ext[:, 2:-2]
    south_c = jnp.where(lat_index == 0, 0.0, north_halo)
    merid_c = jnp.concatenate([south_c, courant_north], axis=0)
    north_flux = face_flux(
        merid_p[0 : n_rows + 1],
        merid_p[1 : n_rows + 2],
        merid_p[2 : n_rows + 3],
        merid_p[3 : n_rows + 4],
        merid_c,
    )
    face_rows = lat_index * n_rows + jnp.arange(-1, n_rows, dtype=jnp.int32)
    cos_face = jnp.sin(
        jnp.minimum(face_rows + 1, n_lat - 1 - face_rows).astype(jnp.float32) * (math.pi / n_lat)
    )
    cell_rows = face_rows[1:]
    cos_cell = jnp.sin(
        (jnp.minimum(cell_rows, n_lat - 1 - cell_rows).astype(jnp.float32) + 0.5)
        * (math.pi / n_lat)
    )
    weighted = cos_face[:, None, None] * north_flux
    meridional = -(weighted[1:] - weighted[:-1]) / cos_cell[:, None, None]
    return centre + zonal + meridional


def solution(mesh):
    placed = (
        P("lat", "lon", None),
        P("lat", "lon", None),
        P("lat", "lon", None),
        P("lat"),
        P("lat"),
    )
    return jax.shard_map(
        local, mesh=mesh, in_specs=placed, out_specs=P("lat", "lon", None), check_vma=False
    )
```

```python
import math

import jax
import jax.numpy as jnp
from jax import lax
from jax.sharding import PartitionSpec as P


def shifted_from(block, axis, distance, wrap=True):
    count = lax.axis_size(axis)
    route = [(i, (i + distance) % count) for i in range(count)]
    if not wrap:
        route = [(i, j) for i, j in route if 0 <= i + distance < count]
    return lax.ppermute(block, axis, route)


def face_flux(far_lo, near_lo, near_hi, far_hi, courant):
    centred = (7.0 * (near_lo + near_hi) - (far_lo + far_hi)) / 12.0
    return courant * centred - 0.5 * jnp.abs(courant) * (near_hi - near_lo)


def build_table(n_full, n_waves, step):
    waves = jnp.arange(n_waves, dtype=jnp.int32)
    coarse = jnp.arange(n_full // step, dtype=jnp.int32) * step
    fine = jnp.arange(step, dtype=jnp.int32)
    scale = 2.0 * math.pi / n_full
    alpha = (coarse[:, None] * waves[None, :] % n_full).astype(jnp.float32) * scale
    beta = (fine[:, None] * waves[None, :] % n_full).astype(jnp.float32) * scale
    ca, sa = jnp.cos(alpha)[:, None], jnp.sin(alpha)[:, None]
    cb, sb = jnp.cos(beta)[None], jnp.sin(beta)[None]
    cos_t = (ca * cb - sa * sb).reshape(n_full, n_waves)
    sin_t = (sa * cb + ca * sb).reshape(n_full, n_waves)
    return jnp.concatenate([cos_t, sin_t], axis=1)


def local(state, courant_east, courant_north, cutoff, filter_mask):
    n_rows, n_cols, n_comp = state.shape
    lon_count = lax.axis_size("lon")
    lat_count = lax.axis_size("lat")
    lat_index = lax.axis_index("lat")
    n_full = n_cols * lon_count
    n_lat = n_rows * lat_count
    half = n_full // 2
    group = n_comp // lon_count
    n_send = n_rows + 5
    n_win = n_cols + 4

    top = n_full // 8 + (half - 1 - n_full // 8) * (n_lat // 4 - 1) // (n_lat // 2)
    n_waves = min(top, half - 1) + 1

    sent = jnp.concatenate([state, courant_north[-1:]], axis=0)
    lead = sent.reshape((n_rows + 1) * n_cols, n_comp).T.reshape(lon_count, -1)
    tail = courant_east[:, -1].T.reshape(lon_count, -1)
    outgoing = jnp.concatenate([lead, tail], axis=1)
    incoming = lax.all_to_all(outgoing, "lon", split_axis=0, concat_axis=0, tiled=True)
    n_lead = group * (n_rows + 1) * n_cols
    lead_in = incoming[:, :n_lead].reshape(lon_count, group, n_rows + 1, n_cols)
    blocks = lead_in[:, :, :n_rows].reshape(lon_count, group * n_rows, n_cols)
    face_row = jnp.transpose(lead_in[:, :, n_rows], (1, 0, 2)).reshape(group, 1, n_full)
    face_col = jnp.roll(incoming[:, n_lead:], 1, axis=0)

    fourier = build_table(n_full, n_waves, 32)
    waves = jnp.arange(n_waves, dtype=jnp.int32)
    weights = jnp.where(waves == 0, 1.0 / n_full, 2.0 / n_full).astype(jnp.float32)
    kept = jnp.where(waves[None, :] <= cutoff[:, None], weights[None, :], 0.0)
    kept_both = jnp.tile(jnp.concatenate([kept, kept], axis=1), (group, 1))
    coeffs = lax.dot_general(
        blocks,
        fourier.reshape(lon_count, n_cols, -1),
        (((0, 2), (0, 1)), ((), ())),
        precision=lax.Precision.HIGH,
    )
    coeffs = coeffs * kept_both
    filtered = lax.dot_general(
        coeffs,
        fourier.reshape(lon_count, n_cols, -1),
        (((1,), (2,)), ((), ())),
        precision=lax.Precision.HIGH,
    )
    keep = jnp.tile(filter_mask, group)[:, None, None] == 1
    smooth = jnp.where(keep, filtered, jnp.transpose(blocks, (1, 0, 2)))
    smooth = smooth.reshape(group, n_rows, n_full)

    from_south = shifted_from(
        jnp.concatenate([smooth[:, -2:], face_row], axis=1), "lat", 1, wrap=False
    )
    from_north = shifted_from(smooth[:, :2], "lat", -1, wrap=False)
    south_pole = jnp.roll(smooth[:, 1::-1], half, axis=2)
    north_pole = jnp.roll(smooth[:, : n_rows - 3 : -1], half, axis=2)
    low = jnp.where(lat_index == 0, south_pole, from_south[:, :2])
    high = jnp.where(lat_index == lat_count - 1, north_pole, from_north)
    rows_out = jnp.concatenate([low, smooth, high, from_south[:, 2:]], axis=1)

    tiles = rows_out.reshape(group, n_send, lon_count, n_cols)
    left = jnp.roll(tiles[..., -2:], 1, axis=2)
    right = jnp.roll(tiles[..., :2], -1, axis=2)
    windows = jnp.concatenate([left, tiles, right], axis=3)
    windows = jnp.transpose(windows, (2, 0, 1, 3)).reshape(lon_count, -1)
    windows = jnp.concatenate([windows, face_col], axis=1)
    back = lax.all_to_all(windows, "lon", split_axis=0, concat_axis=0, tiled=True)
    n_back = group * n_send * n_win
    ext = back[:, :n_back].reshape(n_comp, -1).T.reshape(n_send, n_win, n_comp)
    east_halo = back[:, n_back:].reshape(n_comp, n_rows).T[:, None, :]
    north_halo = ext[n_send - 1 :, 2:-2]
    ext = ext[: n_send - 1]
    own = ext[2:-2]
    centre = own[:, 2:-2]

    zonal_c = jnp.concatenate([east_halo, courant_east], axis=1)
    east = face_flux(
        own[:, 0 : n_cols + 1],
        own[:, 1 : n_cols + 2],
        own[:, 2 : n_cols + 3],
        own[:, 3 : n_cols + 4],
        zonal_c,
    )
    zonal = -(east[:, 1:] - east[:, :-1])

    merid_p = ext[:, 2:-2]
    south_c = jnp.where(lat_index == 0, 0.0, north_halo)
    merid_c = jnp.concatenate([south_c, courant_north], axis=0)
    north_flux = face_flux(
        merid_p[0 : n_rows + 1],
        merid_p[1 : n_rows + 2],
        merid_p[2 : n_rows + 3],
        merid_p[3 : n_rows + 4],
        merid_c,
    )
    face_rows = lat_index * n_rows + jnp.arange(-1, n_rows, dtype=jnp.int32)
    cos_face = jnp.sin(
        jnp.minimum(face_rows + 1, n_lat - 1 - face_rows).astype(jnp.float32) * (math.pi / n_lat)
    )
    cell_rows = face_rows[1:]
    cos_cell = jnp.sin(
        (jnp.minimum(cell_rows, n_lat - 1 - cell_rows).astype(jnp.float32) + 0.5)
        * (math.pi / n_lat)
    )
    weighted = cos_face[:, None, None] * north_flux
    meridional = -(weighted[1:] - weighted[:-1]) / cos_cell[:, None, None]
    return centre + zonal + meridional


def solution(mesh):
    placed = (
        P("lat", "lon", None),
        P("lat", "lon", None),
        P("lat", "lon", None),
        P("lat"),
        P("lat"),
    )
    return jax.shard_map(
        local, mesh=mesh, in_specs=placed, out_specs=P("lat", "lon", None), check_vma=False
    )
```
